256 devices in a mesh: var: 8 (over y, core), tok: 32 (over x, z).
Axes of the slice: x: 4, y: 4, z: 8, core: 2. Of those that a mesh axis runs over, the one named last changes fastest.
Arguments:
- patches: bfloat16 [72, 4, 4096], P('var', None, 'tok'), may hold values from -6 to 6
- slot_var: int32 [72], replicated, may hold values from -1 to 47, as said below
- patch_weight: bfloat16 [48, 4, 1024], replicated, may hold values from -3 to 3
- var_embed: bfloat16 [48, 1024], replicated, may hold values from -6 to 6
- query: bfloat16 [1024], replicated, may hold values from -16 to 16
- key_weight: bfloat16 [1024, 1024], P('tok'), may hold values from -0.1875 to 0.1875
- value_weight: bfloat16 [1024, 1024], P('tok'), may hold values from -0.1875 to 0.1875
- out_weight: bfloat16 [1024, 1024], P('tok'), may hold values from -0.1875 to 0.1875
- cotangent: bfloat16 [4096, 1024], P(('tok', 'var')), may hold values from -6 to 6
Outputs:
- aggregated: bfloat16 [4096, 1024], P(('tok', 'var'))
- patch_grad: float32 [72, 4096], P('var', 'tok')
The draws below stay inside these ranges and needn't reach their ends.
Inputs may be any that keep to these rules, and one draw needn't show every extreme that they name: `slot_var`: slot 9 * i + j belongs to index i of var. Every variable id stands in exactly one slot; empty slots hold -1. The live slots of an index come first and hold consecutive ids, rising from index to index. Every index holds at least one and at most 9 live slots, and some index holds exactly 9.
All inputs are finite; a program needn't handle non-finite values.
Results may differ from the reference program's by a relative error of at most 0.011.
Values may be sent and summed in bfloat16 or wider, within the bound.
No kernel may reach another device: no remote copies, remote signals or barrier semaphores. Data moves between devices by JAX's collectives and lax.ppermute only.
A program may use at most 128 MiB of HBM per device.

```python
import math
import jax
import jax.numpy as jnp
from jax import lax

V = 48
D = 1024
H = 16
HD = 64
VSLOT = 9
SLOTS = 72
TOKENS = 4096
N_VAR = 8


def draw_slot_var(key, part):
    base = V // N_VAR
    extra = VSLOT - base
    order = jax.random.permutation(jax.random.fold_in(key, 11), N_VAR)
    shifts = jax.random.randint(jax.random.fold_in(key, 12), (N_VAR // 2,), 0, extra + 1).astype(jnp.int32)
    shifts = shifts.at[0].set(extra)
    deltas = jnp.concatenate([shifts, -shifts])
    counts = jnp.zeros((N_VAR,), jnp.int32).at[order].set(base + deltas)
    starts = jnp.cumsum(counts) - counts
    slots = jnp.arange(N_VAR * VSLOT, dtype=jnp.int32)
    owner = slots // VSLOT
    within = slots % VSLOT
    return jnp.where(within < counts[owner], starts[owner] + within, -1).astype(jnp.int32)


def block_scale(own_key, shape, cuts, smallest, top_value):
    def one(axis_at, blocks):
        heights = jax.random.uniform(jax.random.fold_in(jax.random.fold_in(own_key, 6), axis_at), (blocks,), jnp.float32, smallest / len(cuts), top_value / len(cuts))
        return jnp.repeat(jnp.exp(heights), shape[axis_at] // blocks).reshape((-1,) + (1,) * (len(shape) - axis_at - 1))

    loudness = one(*cuts[0])
    for cut in cuts[1:]:
        loudness = loudness * one(*cut)
    return loudness


def normal_values(key, dims, scale, most, shards=(), kind=jnp.bfloat16):
    result = jax.random.normal(key, dims, jnp.float32) * scale
    if len(shards) > 0:
        result = block_scale(key, dims, shards, -0.22, 0.18) * result
    return jnp.clip(result, min=-most, max=most).astype(kind)


def setup_inputs(seed: int = 0) -> dict:
    key_of = jax.random.split(jax.random.key(seed), 10)
    return {
        "patches": normal_values(key_of[0], (SLOTS, 4, TOKENS), 1.0, 6.0, ((0, 8), (2, 32))),
        "slot_var": draw_slot_var(jax.random.fold_in(key_of[9], 71), 0),
        "patch_weight": normal_values(key_of[2], (V, 4, D), 4 ** -0.5, 3.0),
        "var_embed": normal_values(key_of[3], (V, D), 1.0, 6.0),
        "query": normal_values(key_of[4], (D,), 4.0, 16.0),
        "key_weight": normal_values(key_of[5], (D, D), D ** -0.5, 0.1875, ((0, 32),)),
        "value_weight": normal_values(key_of[6], (D, D), D ** -0.5, 0.1875, ((0, 32),)),
        "out_weight": normal_values(key_of[7], (D, D), D ** -0.5, 0.1875, ((0, 32),)),
        "cotangent": normal_values(key_of[8], (TOKENS, D), 1.0, 6.0, ((0, 256),)),
    }


score_cap = 5.0
inv_sqrt_two = 1.0 / math.sqrt(2.0)
inv_sqrt_two_pi = 1.0 / math.sqrt(2.0 * math.pi)

def gelu_exact(inputs):
    return 0.5 * inputs * (1.0 + lax.erf(inputs * inv_sqrt_two))

def gelu_slope(inputs):
    return 0.5 * (1.0 + lax.erf(inputs * inv_sqrt_two)) + inputs * jnp.exp(-0.5 * inputs * inputs) * inv_sqrt_two_pi

def live_index(slot_var):
    ids = jnp.arange(V, dtype=jnp.int32)
    places = jnp.arange(slot_var.shape[0], dtype=jnp.int32)
    match = slot_var[None, :] == ids[:, None]
    return lax.optimization_barrier(jnp.sum(jnp.where(match, places[None, :], 0), axis=1)).astype(jnp.int32)

def attend(embedded, query, key_weight, value_weight, out_weight, cot_rows):
    var_count, tok_count, width = embedded.shape
    flat_rows = embedded.reshape(var_count * tok_count, width)
    key_heads = jnp.dot(flat_rows, key_weight, preferred_element_type=jnp.float32).astype(jnp.bfloat16).reshape(var_count, tok_count, H, HD)
    value_heads = jnp.dot(flat_rows, value_weight, preferred_element_type=jnp.float32).astype(jnp.bfloat16).reshape(var_count, tok_count, H, HD)
    query_heads = query.reshape(H, HD).astype(jnp.float32)
    raw_scores = jnp.einsum('vthj,hj->tvh', key_heads.astype(jnp.float32), query_heads) / math.sqrt(HD)
    squashed = jnp.tanh(raw_scores / score_cap)
    exp_scores = jnp.exp(score_cap * squashed)
    attn_f32 = exp_scores / lax.optimization_barrier(jnp.sum(exp_scores, axis=1, keepdims=True))
    attn_bf = attn_f32.astype(jnp.bfloat16)
    pooled = jnp.einsum('tvh,vthj->thj', attn_bf.astype(jnp.float32), value_heads.astype(jnp.float32)).astype(jnp.bfloat16).reshape(tok_count, width)
    mixed = jnp.dot(pooled, out_weight, preferred_element_type=jnp.float32).astype(jnp.bfloat16)
    grad_pooled = jnp.dot(cot_rows, out_weight.T, preferred_element_type=jnp.float32).astype(jnp.bfloat16).reshape(tok_count, H, HD)
    grad_attn = jnp.einsum('thj,vthj->tvh', grad_pooled.astype(jnp.float32), value_heads.astype(jnp.float32))
    attn_vth = jnp.transpose(attn_bf, (1, 0, 2)).astype(jnp.float32)
    grad_values = (attn_vth[:, :, :, None] * grad_pooled.astype(jnp.float32)[None]).astype(jnp.bfloat16)
    grad_scores = attn_f32 * (grad_attn - lax.optimization_barrier(jnp.sum(attn_f32 * grad_attn, axis=1, keepdims=True)))
    grad_raw = grad_scores * (1.0 - squashed * squashed) / math.sqrt(HD)
    grad_keys = (jnp.transpose(grad_raw, (1, 0, 2))[:, :, :, None] * query_heads[None, None]).astype(jnp.bfloat16)
    grad_embed = jnp.dot(grad_keys.reshape(var_count * tok_count, width), key_weight.T, preferred_element_type=jnp.float32)
    grad_embed = grad_embed + jnp.dot(grad_values.reshape(var_count * tok_count, width), value_weight.T, preferred_element_type=jnp.float32)
    return (mixed, grad_embed.astype(jnp.bfloat16).reshape(var_count, tok_count, width))

def reference(patches, slot_var, patch_weight, var_embed, query, key_weight, value_weight, out_weight, cotangent):
    live_slot = live_index(slot_var)
    live_pixels = jnp.take(patches, live_slot, axis=0)
    block = math.gcd(TOKENS, 256)
    count = TOKENS // block
    embed_f32 = var_embed.astype(jnp.float32)

    def one_block(carry, index):
        first_tok = (index * block).astype(jnp.int32)
        block_pixels = lax.dynamic_slice_in_dim(live_pixels, first_tok, block, 2)
        cot_rows = lax.dynamic_slice_in_dim(cotangent, first_tok, block, 0)
        pre_act = jnp.einsum('vpt,vpd->vtd', block_pixels, patch_weight, preferred_element_type=jnp.float32) + embed_f32[:, None, :]
        embedded = gelu_exact(pre_act).astype(jnp.bfloat16)
        mixed, grad_embed = attend(embedded, query, key_weight, value_weight, out_weight, cot_rows)
        grad_pre = grad_embed.astype(jnp.float32) * gelu_slope(pre_act)
        carry = carry + jnp.einsum('vpt,vtd->vpd', block_pixels.astype(jnp.float32), grad_pre, precision=lax.Precision.HIGHEST)
        return (carry, mixed)
    total, mixed_all = lax.scan(one_block, jnp.zeros((V, 4, D), jnp.float32), jnp.arange(count, dtype=jnp.int32))
    aggregated = mixed_all.reshape(TOKENS, D)
    patch_grad = jnp.zeros((SLOTS, 4 * D), jnp.float32).at[live_slot].set(total.reshape(V, 4 * D))
    return (aggregated, patch_grad)
```

```python
import math

import jax
import jax.numpy as jnp
from jax import lax
from jax.sharding import PartitionSpec as P

H = 16
HD = 64


score_cap = 5.0
inv_sqrt_two = 1.0 / math.sqrt(2.0)
inv_sqrt_two_pi = 1.0 / math.sqrt(2.0 * math.pi)

f32 = jnp.float32
bf16 = jnp.bfloat16


def gelu_exact(inputs):
    return 0.5 * inputs * (1.0 + lax.erf(inputs * inv_sqrt_two))


def gelu_slope(inputs):
    return (
        0.5 * (1.0 + lax.erf(inputs * inv_sqrt_two))
        + inputs * jnp.exp(-0.5 * inputs * inputs) * inv_sqrt_two_pi
    )


def live_index(slot_var, var_total):
    ids = jnp.arange(var_total, dtype=jnp.int32)
    places = jnp.arange(slot_var.shape[0], dtype=jnp.int32)
    match = slot_var[None, :] == ids[:, None]
    return jnp.sum(jnp.where(match, places[None, :], 0), axis=1)


def split(x):
    hi = x.astype(bf16)
    lo = (x - hi.astype(f32)).astype(bf16)
    return hi, lo


def ein(spec, a, b):
    return jnp.einsum(spec, a, b, preferred_element_type=f32)


def body(
    patches,
    slot_var,
    patch_weight,
    var_embed,
    query,
    key_weight,
    value_weight,
    out_weight,
    cotangent,
    *,
    n_var,
    n_tok,
):
    var_total, pixels_per, width = patch_weight.shape
    local_slots = patches.shape[0]
    rows = key_weight.shape[0]
    tok_count = cotangent.shape[0]

    query_heads = query.reshape(H, HD).astype(f32)
    wq_rows = jnp.sum(key_weight.reshape(rows, H, HD).astype(f32) * query_heads[None], axis=2)
    wq_hi, wq_lo = split(wq_rows)
    pad = (-(2 * width + 2 * H)) % 128
    packed = jnp.concatenate(
        [value_weight, out_weight, wq_hi, wq_lo, jnp.zeros((rows, pad), bf16)], axis=1
    )
    full = lax.all_gather(packed, "tok", axis=0, tiled=True)
    value_matrix = full[:, :width]
    out_matrix = full[:, width : 2 * width]
    wq_hi = full[:, 2 * width : 2 * width + H]
    wq_lo = full[:, 2 * width + H : 2 * width + 2 * H]

    slot_pixels = lax.all_to_all(patches, "var", 2, 0, tiled=True)
    live_slot = live_index(slot_var, var_total)
    pixels = jnp.take(slot_pixels, live_slot, axis=0)
    pre_act = ein("vpt,vpd->vtd", pixels, patch_weight) + var_embed.astype(f32)[:, None, :]
    embedded = gelu_exact(pre_act).astype(bf16)

    raw_scores = (ein("vtd,dh->tvh", embedded, wq_hi) + ein("vtd,dh->tvh", embedded, wq_lo)) / math.sqrt(HD)
    squashed = jnp.tanh(raw_scores / score_cap)
    exp_scores = jnp.exp(score_cap * squashed)
    attn_f32 = exp_scores / jnp.sum(exp_scores, axis=1, keepdims=True)
    attn_bf = attn_f32.astype(bf16)

    value_heads = value_matrix.reshape(width, H, HD)
    mixed_in = ein("tvh,vtd->thd", attn_bf, embedded)
    mix_hi, mix_lo = split(mixed_in)
    pooled = (
        (ein("thd,dhj->thj", mix_hi, value_heads) + ein("thd,dhj->thj", mix_lo, value_heads))
        .astype(bf16)
        .reshape(tok_count, width)
    )
    mixed_out = jnp.dot(pooled, out_matrix, preferred_element_type=f32).astype(bf16)
    contract = (((1,), (1,)), ((), ()))
    grad_pooled = (
        lax.dot_general(cotangent, out_matrix, contract, preferred_element_type=f32)
        .astype(bf16)
        .reshape(tok_count, H, HD)
    )
    spread = ein("thj,dhj->thd", grad_pooled, value_heads)
    spread_hi, spread_lo = split(spread)
    grad_attn = ein("vtd,thd->tvh", embedded, spread_hi) + ein("vtd,thd->tvh", embedded, spread_lo)
    grad_scores = attn_f32 * (grad_attn - jnp.sum(attn_f32 * grad_attn, axis=1, keepdims=True))
    grad_raw = grad_scores * (1.0 - squashed * squashed) / math.sqrt(HD)
    raw_hi, raw_lo = split(grad_raw)
    grad_embed = (
        ein("tvh,thd->vtd", attn_bf, spread_hi)
        + ein("tvh,thd->vtd", attn_bf, spread_lo)
        + ein("tvh,dh->vtd", raw_hi, wq_hi)
        + ein("tvh,dh->vtd", raw_hi, wq_lo)
        + ein("tvh,dh->vtd", raw_lo, wq_hi)
    ).astype(bf16)
    grad_pre = grad_embed.astype(f32) * gelu_slope(pre_act)
    partial = jnp.einsum(
        "vpt,vtd->vpd", pixels.astype(f32), grad_pre, precision=lax.Precision.HIGHEST
    ).reshape(var_total, pixels_per * width)

    slots = n_var * local_slots
    cols = partial.shape[1] // n_tok
    safe = jnp.clip(slot_var, 0, var_total - 1)
    slot_rows = jnp.where((slot_var >= 0)[:, None], jnp.take(partial, safe, axis=0), 0.0)
    blocks = slot_rows.reshape(n_var, local_slots, n_tok, cols).transpose(0, 2, 1, 3)
    by_var = lax.all_to_all(blocks, "var", 0, 0, tiled=True).sum(axis=0)
    by_tok = lax.all_to_all(by_var, "tok", 0, 0, tiled=True).sum(axis=0)
    del slots
    return (mixed_out, by_tok)


def solution(mesh):
    import functools

    fn = functools.partial(body, n_var=mesh.shape["var"], n_tok=mesh.shape["tok"])
    return jax.shard_map(
        fn,
        mesh=mesh,
        in_specs=(
            P("var", None, "tok"),
            P(),
            P(),
            P(),
            P(),
            P("tok", None),
            P("tok", None),
            P("tok", None),
            P(("tok", "var"), None),
        ),
        out_specs=(P(("tok", "var"), None), P("var", "tok")),
        check_vma=False,
    )
```

```python
import math

import jax
import jax.numpy as jnp
from jax import lax
from jax.sharding import PartitionSpec as P

H = 16
HD = 64


score_cap = 5.0
inv_sqrt_two = 1.0 / math.sqrt(2.0)
inv_sqrt_two_pi = 1.0 / math.sqrt(2.0 * math.pi)

f32 = jnp.float32
bf16 = jnp.bfloat16


def gelu_exact(inputs):
    return 0.5 * inputs * (1.0 + lax.erf(inputs * inv_sqrt_two))


def gelu_slope(inputs):
    return (
        0.5 * (1.0 + lax.erf(inputs * inv_sqrt_two))
        + inputs * jnp.exp(-0.5 * inputs * inputs) * inv_sqrt_two_pi
    )


def live_index(slot_var, var_total):
    ids = jnp.arange(var_total, dtype=jnp.int32)
    places = jnp.arange(slot_var.shape[0], dtype=jnp.int32)
    match = slot_var[None, :] == ids[:, None]
    return jnp.sum(jnp.where(match, places[None, :], 0), axis=1)


def split(x):
    hi = x.astype(bf16)
    lo = (x - hi.astype(f32)).astype(bf16)
    return hi, lo


def ein(spec, a, b):
    return jnp.einsum(spec, a, b, preferred_element_type=f32)


def body(
    patches,
    slot_var,
    patch_weight,
    var_embed,
    query,
    key_weight,
    value_weight,
    out_weight,
    cotangent,
    *,
    n_var,
    n_tok,
):
    var_total, pixels_per, width = patch_weight.shape
    local_slots = patches.shape[0]
    rows = key_weight.shape[0]
    tok_count = cotangent.shape[0]

    query_heads = query.reshape(H, HD).astype(f32)
    wq_rows = jnp.sum(key_weight.reshape(rows, H, HD).astype(f32) * query_heads[None], axis=2)
    wq_copies = jnp.broadcast_to(wq_rows[None], (n_tok, rows, H))
    wq_full = lax.all_to_all(wq_copies, "tok", 0, 0, tiled=True).reshape(n_tok * rows, H)
    wq_hi, wq_lo = split(wq_full)
    full = lax.all_gather(jnp.stack([value_weight, out_weight]), "tok", axis=1, tiled=True)
    value_matrix = full[0]
    out_matrix = full[1]

    slot_pixels = lax.all_to_all(patches, "var", 2, 0, tiled=True)
    live_slot = live_index(slot_var, var_total)
    pixels = jnp.take(slot_pixels, live_slot, axis=0)
    pre_act = ein("vpt,vpd->vtd", pixels, patch_weight) + var_embed.astype(f32)[:, None, :]
    embedded = gelu_exact(pre_act).astype(bf16)

    raw_scores = (ein("vtd,dh->tvh", embedded, wq_hi) + ein("vtd,dh->tvh", embedded, wq_lo)) / math.sqrt(HD)
    squashed = jnp.tanh(raw_scores / score_cap)
    exp_scores = jnp.exp(score_cap * squashed)
    attn_f32 = exp_scores / jnp.sum(exp_scores, axis=1, keepdims=True)
    attn_bf = attn_f32.astype(bf16)

    value_heads = value_matrix.reshape(width, H, HD)
    mixed_in = ein("tvh,vtd->thd", attn_bf, embedded)
    mix_hi, mix_lo = split(mixed_in)
    pooled = (
        (ein("thd,dhj->thj", mix_hi, value_heads) + ein("thd,dhj->thj", mix_lo, value_heads))
        .astype(bf16)
        .reshape(tok_count, width)
    )
    mixed_out = jnp.dot(pooled, out_matrix, preferred_element_type=f32).astype(bf16)
    contract = (((1,), (1,)), ((), ()))
    grad_pooled = (
        lax.dot_general(cotangent, out_matrix, contract, preferred_element_type=f32)
        .astype(bf16)
        .reshape(tok_count, H, HD)
    )
    spread = ein("thj,dhj->thd", grad_pooled, value_heads)
    spread_hi, spread_lo = split(spread)
    grad_attn = ein("vtd,thd->tvh", embedded, spread_hi) + ein("vtd,thd->tvh", embedded, spread_lo)
    grad_scores = attn_f32 * (grad_attn - jnp.sum(attn_f32 * grad_attn, axis=1, keepdims=True))
    grad_raw = grad_scores * (1.0 - squashed * squashed) / math.sqrt(HD)
    raw_hi, raw_lo = split(grad_raw)
    grad_embed = (
        ein("tvh,thd->vtd", attn_bf, spread_hi)
        + ein("tvh,thd->vtd", attn_bf, spread_lo)
        + ein("tvh,dh->vtd", raw_hi, wq_hi)
        + ein("tvh,dh->vtd", raw_hi, wq_lo)
        + ein("tvh,dh->vtd", raw_lo, wq_hi)
    ).astype(bf16)
    grad_pre = grad_embed.astype(f32) * gelu_slope(pre_act)
    partial = jnp.einsum(
        "vpt,vtd->vpd", pixels.astype(f32), grad_pre, precision=lax.Precision.HIGHEST
    ).reshape(var_total, pixels_per * width)

    slots = n_var * local_slots
    cols = partial.shape[1] // n_tok
    safe = jnp.clip(slot_var, 0, var_total - 1)
    slot_rows = jnp.where((slot_var >= 0)[:, None], jnp.take(partial, safe, axis=0), 0.0)
    blocks = slot_rows.reshape(n_var, local_slots, n_tok, cols).transpose(0, 2, 1, 3)
    by_var = lax.all_to_all(blocks, "var", 0, 0, tiled=True).sum(axis=0)
    by_tok = lax.all_to_all(by_var, "tok", 0, 0, tiled=True).sum(axis=0)
    del slots
    return (mixed_out, by_tok)


def solution(mesh):
    import functools

    fn = functools.partial(body, n_var=mesh.shape["var"], n_tok=mesh.shape["tok"])
    return jax.shard_map(
        fn,
        mesh=mesh,
        in_specs=(
            P("var", None, "tok"),
            P(),
            P(),
            P(),
            P(),
            P("tok", None),
            P("tok", None),
            P("tok", None),
            P(("tok", "var"), None),
        ),
        out_specs=(P(("tok", "var"), None), P("var", "tok")),
        check_vma=False,
    )
```

```python
import math

import jax
import jax.numpy as jnp
from jax import lax
from jax.sharding import PartitionSpec as P

H = 16
HD = 64


score_cap = 5.0
inv_sqrt_two = 1.0 / math.sqrt(2.0)
inv_sqrt_two_pi = 1.0 / math.sqrt(2.0 * math.pi)

f32 = jnp.float32
bf16 = jnp.bfloat16


def gelu_exact(inputs):
    return 0.5 * inputs * (1.0 + lax.erf(inputs * inv_sqrt_two))


def gelu_slope(inputs):
    return (
        0.5 * (1.0 + lax.erf(inputs * inv_sqrt_two))
        + inputs * jnp.exp(-0.5 * inputs * inputs) * inv_sqrt_two_pi
    )


def live_index(slot_var, var_total):
    ids = jnp.arange(var_total, dtype=jnp.int32)
    places = jnp.arange(slot_var.shape[0], dtype=jnp.int32)
    match = slot_var[None, :] == ids[:, None]
    return jnp.sum(jnp.where(match, places[None, :], 0), axis=1)


def split(x):
    hi = x.astype(bf16)
    lo = (x - hi.astype(f32)).astype(bf16)
    return hi, lo


def ein(spec, a, b):
    return jnp.einsum(spec, a, b, preferred_element_type=f32)


def body(
    patches,
    slot_var,
    patch_weight,
    var_embed,
    query,
    key_weight,
    value_weight,
    out_weight,
    cotangent,
    *,
    n_var,
    n_tok,
):
    var_total, pixels_per, width = patch_weight.shape
    local_slots = patches.shape[0]
    rows = key_weight.shape[0]
    tok_count = cotangent.shape[0]

    query_heads = query.reshape(H, HD).astype(f32)
    wq_rows = jnp.sum(key_weight.reshape(rows, H, HD).astype(f32) * query_heads[None], axis=2)
    wq_copies = jnp.broadcast_to(wq_rows[None], (n_tok, rows, H))
    wq_full = lax.all_to_all(wq_copies, "tok", 0, 0, tiled=True).reshape(n_tok * rows, H)
    wq_hi, wq_lo = split(wq_full)
    full = lax.all_gather(jnp.stack([value_weight, out_weight]), "tok", axis=1, tiled=True)
    value_matrix = full[0]
    out_matrix = full[1]

    slot_pixels = lax.all_to_all(patches, "var", 2, 0, tiled=True)
    live_slot = live_index(slot_var, var_total)
    pixels = jnp.take(slot_pixels, live_slot, axis=0)
    pre_act = ein("vpt,vpd->vtd", pixels, patch_weight) + var_embed.astype(f32)[:, None, :]
    embedded = gelu_exact(pre_act).astype(bf16)

    raw_scores = (ein("vtd,dh->tvh", embedded, wq_hi) + ein("vtd,dh->tvh", embedded, wq_lo)) / math.sqrt(HD)
    squashed = jnp.tanh(raw_scores / score_cap)
    exp_scores = jnp.exp(score_cap * squashed)
    attn_f32 = exp_scores / jnp.sum(exp_scores, axis=1, keepdims=True)
    attn_bf = attn_f32.astype(bf16)

    value_heads = value_matrix.reshape(width, H, HD)
    mixed_in = ein("tvh,vtd->thd", attn_bf, embedded)
    mix_hi, mix_lo = split(mixed_in)
    pooled = (
        (ein("thd,dhj->thj", mix_hi, value_heads) + ein("thd,dhj->thj", mix_lo, value_heads))
        .astype(bf16)
        .reshape(tok_count, width)
    )
    mixed_out = jnp.dot(pooled, out_matrix, preferred_element_type=f32).astype(bf16)
    contract = (((1,), (1,)), ((), ()))
    grad_pooled = (
        lax.dot_general(out_matrix, cotangent, contract, preferred_element_type=f32)
        .T.astype(bf16)
        .reshape(tok_count, H, HD)
    )
    spread = ein("thj,dhj->thd", grad_pooled, value_heads)
    spread_hi, spread_lo = split(spread)
    both = ein("vtd,thd->tvh", embedded, jnp.concatenate([spread_hi, spread_lo], axis=1))
    grad_attn = both[:, :, :H] + both[:, :, H:]
    grad_scores = attn_f32 * (grad_attn - jnp.sum(attn_f32 * grad_attn, axis=1, keepdims=True))
    grad_raw = grad_scores * (1.0 - squashed * squashed) / math.sqrt(HD)
    raw_hi, raw_lo = split(grad_raw)
    left = jnp.concatenate([attn_bf, attn_bf, raw_hi, raw_hi, raw_lo], axis=2)
    wq_t = jnp.concatenate([wq_hi.T, wq_lo.T, wq_hi.T], axis=0)
    right = jnp.concatenate(
        [spread_hi, spread_lo, jnp.broadcast_to(wq_t[None], (tok_count,) + wq_t.shape)], axis=1
    )
    grad_embed = ein("tvk,tkd->vtd", left, right).astype(bf16)
    grad_pre = grad_embed.astype(f32) * gelu_slope(pre_act)
    partial = jnp.einsum(
        "vpt,vtd->vpd", pixels.astype(f32), grad_pre, precision=lax.Precision.HIGHEST
    ).reshape(var_total, pixels_per * width)

    slots = n_var * local_slots
    cols = partial.shape[1] // n_tok
    safe = jnp.clip(slot_var, 0, var_total - 1)
    slot_rows = jnp.where((slot_var >= 0)[:, None], jnp.take(partial, safe, axis=0), 0.0)
    blocks = slot_rows.reshape(n_var, local_slots, n_tok, cols).transpose(0, 2, 1, 3)
    by_var = lax.all_to_all(blocks, "var", 0, 0, tiled=True).sum(axis=0)
    by_tok = lax.all_to_all(by_var, "tok", 0, 0, tiled=True).sum(axis=0)
    del slots
    return (mixed_out, by_tok)


def solution(mesh):
    import functools

    fn = functools.partial(body, n_var=mesh.shape["var"], n_tok=mesh.shape["tok"])
    return jax.shard_map(
        fn,
        mesh=mesh,
        in_specs=(
            P("var", None, "tok"),
            P(),
            P(),
            P(),
            P(),
            P("tok", None),
            P("tok", None),
            P("tok", None),
            P(("tok", "var"), None),
        ),
        out_specs=(P(("tok", "var"), None), P("var", "tok")),
        check_vma=False,
    )
```

```python
import math

import jax
import jax.numpy as jnp
from jax import lax
from jax.sharding import PartitionSpec as P

H = 16
HD = 64


score_cap = 5.0
inv_sqrt_two = 1.0 / math.sqrt(2.0)
inv_sqrt_two_pi = 1.0 / math.sqrt(2.0 * math.pi)

f32 = jnp.float32
bf16 = jnp.bfloat16


def gelu_exact(inputs):
    return 0.5 * inputs * (1.0 + lax.erf(inputs * inv_sqrt_two))


def gelu_slope(inputs):
    return (
        0.5 * (1.0 + lax.erf(inputs * inv_sqrt_two))
        + inputs * jnp.exp(-0.5 * inputs * inputs) * inv_sqrt_two_pi
    )


def live_index(slot_var, var_total):
    ids = jnp.arange(var_total, dtype=jnp.int32)
    places = jnp.arange(slot_var.shape[0], dtype=jnp.int32)
    match = slot_var[None, :] == ids[:, None]
    return jnp.sum(jnp.where(match, places[None, :], 0), axis=1)


def split(x):
    hi = x.astype(bf16)
    lo = (x - hi.astype(f32)).astype(bf16)
    return hi, lo


def ein(spec, a, b):
    return jnp.einsum(spec, a, b, preferred_element_type=f32)


def body(
    patches,
    slot_var,
    patch_weight,
    var_embed,
    query,
    key_weight,
    value_weight,
    out_weight,
    cotangent,
    *,
    n_var,
    n_tok,
):
    var_total, pixels_per, width = patch_weight.shape
    local_slots = patches.shape[0]
    rows = key_weight.shape[0]
    tok_count = cotangent.shape[0]

    query_heads = query.reshape(H, HD).astype(f32)
    wq_rows = jnp.sum(key_weight.reshape(rows, H, HD).astype(f32) * query_heads[None], axis=2)
    wq_copies = jnp.broadcast_to(wq_rows[None], (n_tok, rows, H))
    wq_full = lax.all_to_all(wq_copies, "tok", 0, 0, tiled=True).reshape(n_tok * rows, H)
    wq_hi, wq_lo = split(wq_full)
    full = lax.all_gather(jnp.stack([value_weight, out_weight]), "tok", axis=1, tiled=True)
    value_matrix = full[0]
    out_matrix = full[1]

    slot_pixels = lax.all_to_all(patches, "var", 2, 0, tiled=True)
    live_slot = live_index(slot_var, var_total)
    pixels = jnp.take(slot_pixels, live_slot, axis=0)
    pre_act = ein("vpt,vpd->vtd", pixels, patch_weight) + var_embed.astype(f32)[:, None, :]
    embedded = gelu_exact(pre_act).astype(bf16)
    slope = lax.optimization_barrier(gelu_slope(pre_act))

    raw_scores = (ein("vtd,dh->tvh", embedded, wq_hi) + ein("vtd,dh->tvh", embedded, wq_lo)) / math.sqrt(HD)
    squashed = jnp.tanh(raw_scores / score_cap)
    exp_scores = jnp.exp(score_cap * squashed)
    attn_f32 = exp_scores / jnp.sum(exp_scores, axis=1, keepdims=True)
    attn_bf = attn_f32.astype(bf16)

    value_heads = value_matrix.reshape(width, H, HD)
    mixed_in = ein("tvh,vtd->thd", attn_bf, embedded)
    mix_hi, mix_lo = split(mixed_in)
    pooled = (
        (ein("thd,dhj->thj", mix_hi, value_heads) + ein("thd,dhj->thj", mix_lo, value_heads))
        .astype(bf16)
        .reshape(tok_count, width)
    )
    mixed_out = jnp.dot(pooled, out_matrix, preferred_element_type=f32).astype(bf16)
    cot_t = lax.optimization_barrier(cotangent.T)
    grad_pooled = (
        jnp.dot(out_matrix, cot_t, preferred_element_type=f32)
        .T.astype(bf16)
        .reshape(tok_count, H, HD)
    )
    spread = ein("thj,dhj->thd", grad_pooled, value_heads)
    spread_hi, spread_lo = split(spread)
    both = ein("vtd,thd->tvh", embedded, jnp.concatenate([spread_hi, spread_lo], axis=1))
    grad_attn = both[:, :, :H] + both[:, :, H:]
    grad_scores = attn_f32 * (grad_attn - jnp.sum(attn_f32 * grad_attn, axis=1, keepdims=True))
    grad_raw = grad_scores * (1.0 - squashed * squashed) / math.sqrt(HD)
    raw_hi, raw_lo = split(grad_raw)
    left = jnp.concatenate([attn_bf, attn_bf, raw_hi, raw_hi, raw_lo], axis=2)
    wq_t = jnp.concatenate([wq_hi.T, wq_lo.T, wq_hi.T], axis=0)
    right = jnp.concatenate(
        [spread_hi, spread_lo, jnp.broadcast_to(wq_t[None], (tok_count,) + wq_t.shape)], axis=1
    )
    grad_embed = ein("tvk,tkd->vtd", left, right).astype(bf16)
    grad_pre = grad_embed.astype(f32) * slope
    partial = jnp.einsum(
        "vpt,vtd->vpd", pixels.astype(f32), grad_pre, precision=lax.Precision.HIGHEST
    ).reshape(var_total, pixels_per * width)

    slots = n_var * local_slots
    cols = partial.shape[1] // n_tok
    safe = jnp.clip(slot_var, 0, var_total - 1)
    slot_rows = jnp.where((slot_var >= 0)[:, None], jnp.take(partial, safe, axis=0), 0.0)
    blocks = slot_rows.reshape(n_var, local_slots, n_tok, cols)
    by_var = lax.all_to_all(blocks, "var", 0, 0, tiled=True).sum(axis=0)
    by_tok = lax.all_to_all(by_var.transpose(1, 0, 2), "tok", 0, 0, tiled=True).sum(axis=0)
    del slots
    return (mixed_out, by_tok)


def solution(mesh):
    import functools

    fn = functools.partial(body, n_var=mesh.shape["var"], n_tok=mesh.shape["tok"])
    return jax.shard_map(
        fn,
        mesh=mesh,
        in_specs=(
            P("var", None, "tok"),
            P(),
            P(),
            P(),
            P(),
            P("tok", None),
            P("tok", None),
            P("tok", None),
            P(("tok", "var"), None),
        ),
        out_specs=(P(("tok", "var"), None), P("var", "tok")),
        check_vma=False,
    )
```

```python
import math

import jax
import jax.numpy as jnp
from jax import lax
from jax.sharding import PartitionSpec as P

H = 16
HD = 64


score_cap = 5.0
inv_sqrt_two = 1.0 / math.sqrt(2.0)
inv_sqrt_two_pi = 1.0 / math.sqrt(2.0 * math.pi)

f32 = jnp.float32
bf16 = jnp.bfloat16


def gelu_exact(inputs):
    return 0.5 * inputs * (1.0 + lax.erf(inputs * inv_sqrt_two))


def gelu_slope(inputs):
    return (
        0.5 * (1.0 + lax.erf(inputs * inv_sqrt_two))
        + inputs * jnp.exp(-0.5 * inputs * inputs) * inv_sqrt_two_pi
    )


def live_index(slot_var, var_total):
    ids = jnp.arange(var_total, dtype=jnp.int32)
    places = jnp.arange(slot_var.shape[0], dtype=jnp.int32)
    match = slot_var[None, :] == ids[:, None]
    return jnp.sum(jnp.where(match, places[None, :], 0), axis=1)


def split(x):
    hi = x.astype(bf16)
    lo = (x - hi.astype(f32)).astype(bf16)
    return hi, lo


def ein(spec, a, b):
    return jnp.einsum(spec, a, b, preferred_element_type=f32)


def body(
    patches,
    slot_var,
    patch_weight,
    var_embed,
    query,
    key_weight,
    value_weight,
    out_weight,
    cotangent,
    *,
    n_var,
    n_tok,
):
    var_total, pixels_per, width = patch_weight.shape
    local_slots = patches.shape[0]
    rows = key_weight.shape[0]
    tok_count = cotangent.shape[0]

    query_heads = query.reshape(H, HD).astype(f32)
    wq_rows = jnp.sum(key_weight.reshape(rows, H, HD).astype(f32) * query_heads[None], axis=2)
    wq_copies = jnp.broadcast_to(wq_rows[None], (n_tok, rows, H))
    wq_full = lax.all_to_all(wq_copies, "tok", 0, 0, tiled=True).reshape(n_tok * rows, H)
    wq_hi, wq_lo = split(wq_full)
    full = lax.all_gather(jnp.stack([value_weight, out_weight]), "tok", axis=1, tiled=True)
    value_matrix = full[0]
    out_matrix = full[1]

    slot_pixels = lax.all_to_all(patches, "var", 2, 0, tiled=True)
    live_slot = live_index(slot_var, var_total)
    pixels = jnp.take(slot_pixels, live_slot, axis=0)
    pre_act = ein("vpt,vpd->vtd", pixels, patch_weight) + var_embed.astype(f32)[:, None, :]
    embedded = gelu_exact(pre_act).astype(bf16)
    slope = lax.optimization_barrier(gelu_slope(pre_act))

    raw_scores = (ein("vtd,dh->tvh", embedded, wq_hi) + ein("vtd,dh->tvh", embedded, wq_lo)) / math.sqrt(HD)
    squashed = jnp.tanh(raw_scores / score_cap)
    exp_scores = jnp.exp(score_cap * squashed)
    attn_f32 = exp_scores / jnp.sum(exp_scores, axis=1, keepdims=True)
    attn_bf = attn_f32.astype(bf16)

    same_head = jnp.arange(H)[:, None] == jnp.arange(H)[None, :]
    mixed_in = ein("tvh,vtd->thd", attn_bf, embedded)
    mix_hi, mix_lo = split(mixed_in)
    rows_both = jnp.concatenate([mix_hi, mix_lo], axis=0).reshape(2 * tok_count * H, width)
    all_heads = jnp.dot(rows_both, value_matrix, preferred_element_type=f32).reshape(2, tok_count, H, H, HD)
    pooled = (
        jnp.sum(jnp.where(same_head[None, None, :, :, None], all_heads, 0.0), axis=(0, 3))
        .astype(bf16)
        .reshape(tok_count, width)
    )
    mixed_out = jnp.dot(pooled, out_matrix, preferred_element_type=f32).astype(bf16)
    cot_t = lax.optimization_barrier(cotangent.T)
    grad_pooled = (
        jnp.dot(out_matrix, cot_t, preferred_element_type=f32)
        .T.astype(bf16)
        .reshape(tok_count, H, HD)
    )
    by_head = jnp.where(same_head[:, None, None, :], grad_pooled.transpose(1, 2, 0)[:, :, :, None], 0)
    spread_t = jnp.dot(value_matrix, by_head.reshape(width, tok_count * H).astype(bf16), preferred_element_type=f32)
    spread = spread_t.reshape(width, tok_count, H).transpose(1, 2, 0)
    spread_hi, spread_lo = split(spread)
    both = ein("vtd,thd->tvh", embedded, jnp.concatenate([spread_hi, spread_lo], axis=1))
    grad_attn = both[:, :, :H] + both[:, :, H:]
    grad_scores = attn_f32 * (grad_attn - jnp.sum(attn_f32 * grad_attn, axis=1, keepdims=True))
    grad_raw = grad_scores * (1.0 - squashed * squashed) / math.sqrt(HD)
    raw_hi, raw_lo = split(grad_raw)
    left = jnp.concatenate([attn_bf, attn_bf, raw_hi, raw_hi, raw_lo], axis=2)
    wq_t = jnp.concatenate([wq_hi.T, wq_lo.T, wq_hi.T], axis=0)
    right = jnp.concatenate(
        [spread_hi, spread_lo, jnp.broadcast_to(wq_t[None], (tok_count,) + wq_t.shape)], axis=1
    )
    grad_embed = ein("tvk,tkd->vtd", left, right).astype(bf16)
    grad_pre = grad_embed.astype(f32) * slope
    partial = jnp.einsum(
        "vpt,vtd->vpd", pixels.astype(f32), grad_pre, precision=lax.Precision.HIGHEST
    ).reshape(var_total, pixels_per * width)

    slots = n_var * local_slots
    cols = partial.shape[1] // n_tok
    safe = jnp.clip(slot_var, 0, var_total - 1)
    slot_rows = jnp.where((slot_var >= 0)[:, None], jnp.take(partial, safe, axis=0), 0.0)
    blocks = slot_rows.reshape(n_var, local_slots, n_tok, cols)
    by_var = lax.all_to_all(blocks, "var", 0, 0, tiled=True).sum(axis=0)
    by_tok = lax.all_to_all(by_var.transpose(1, 0, 2), "tok", 0, 0, tiled=True).sum(axis=0)
    del slots
    return (mixed_out, by_tok)


def solution(mesh):
    import functools

    fn = functools.partial(body, n_var=mesh.shape["var"], n_tok=mesh.shape["tok"])
    return jax.shard_map(
        fn,
        mesh=mesh,
        in_specs=(
            P("var", None, "tok"),
            P(),
            P(),
            P(),
            P(),
            P("tok", None),
            P("tok", None),
            P("tok", None),
            P(("tok", "var"), None),
        ),
        out_specs=(P(("tok", "var"), None), P("var", "tok")),
        check_vma=False,
    )
```

```python
import math

import jax
import jax.numpy as jnp
from jax import lax
from jax.sharding import PartitionSpec as P

H = 16
HD = 64


score_cap = 5.0
inv_sqrt_two = 1.0 / math.sqrt(2.0)
inv_sqrt_two_pi = 1.0 / math.sqrt(2.0 * math.pi)

f32 = jnp.float32
bf16 = jnp.bfloat16


def gelu_exact(inputs):
    return 0.5 * inputs * (1.0 + lax.erf(inputs * inv_sqrt_two))


def gelu_slope(inputs):
    return (
        0.5 * (1.0 + lax.erf(inputs * inv_sqrt_two))
        + inputs * jnp.exp(-0.5 * inputs * inputs) * inv_sqrt_two_pi
    )


def live_index(slot_var, var_total):
    ids = jnp.arange(var_total, dtype=jnp.int32)
    places = jnp.arange(slot_var.shape[0], dtype=jnp.int32)
    match = slot_var[None, :] == ids[:, None]
    return jnp.sum(jnp.where(match, places[None, :], 0), axis=1)


def split(x):
    hi = x.astype(bf16)
    lo = (x - hi.astype(f32)).astype(bf16)
    return hi, lo


def ein(spec, a, b):
    return jnp.einsum(spec, a, b, preferred_element_type=f32)


def ring_steps(block, n, perm_of):
    forward, backward = block, block
    behind, ahead = [], []
    for k in range(1, n // 2 + 1):
        forward = lax.ppermute(forward, "tok", perm_of(1))
        behind.append(forward)
        if k < n - k:
            backward = lax.ppermute(backward, "tok", perm_of(-1))
            ahead.append(backward)
    return jnp.stack([block] + behind + ahead[::-1])


def ring_gather(block, n_x, n_z):
    def along_z(step):
        return [(x * n_z + z, x * n_z + (z + step) % n_z) for x in range(n_x) for z in range(n_z)]

    def along_x(step):
        return [(x * n_z + z, ((x + step) % n_x) * n_z + z) for x in range(n_x) for z in range(n_z)]

    me = lax.axis_index("tok")
    my_z, my_x = me % n_z, me // n_z
    by_z = ring_steps(block, n_z, along_z)
    by_z = jnp.take(by_z, (my_z - jnp.arange(n_z)) % n_z, axis=0)
    by_x = ring_steps(by_z, n_x, along_x)
    by_x = jnp.take(by_x, (my_x - jnp.arange(n_x)) % n_x, axis=0)
    return by_x.reshape((n_x * n_z * block.shape[0],) + block.shape[1:])


def body(
    patches,
    slot_var,
    patch_weight,
    var_embed,
    query,
    key_weight,
    value_weight,
    out_weight,
    cotangent,
    *,
    n_var,
    n_tok,
    n_tok_x,
    n_tok_z,
):
    var_total, pixels_per, width = patch_weight.shape
    local_slots = patches.shape[0]
    rows = key_weight.shape[0]
    tok_count = cotangent.shape[0]

    query_heads = query.reshape(H, HD).astype(f32)
    wq_rows = jnp.sum(key_weight.reshape(rows, H, HD).astype(f32) * query_heads[None], axis=2)
    wq_copies = jnp.broadcast_to(wq_rows[None], (n_tok, rows, H))
    wq_full = lax.all_to_all(wq_copies, "tok", 0, 0, tiled=True).reshape(n_tok * rows, H)
    wq_hi, wq_lo = split(wq_full)
    core = lax.axis_index("var") % 2
    mine = jnp.where(core == 0, value_weight, out_weight)
    gathered = ring_gather(mine, n_tok_x, n_tok_z)
    other = lax.ppermute(gathered, "var", [(i, i ^ 1) for i in range(n_var)])
    value_matrix = jnp.where(core == 0, gathered, other)
    out_matrix = jnp.where(core == 0, other, gathered)

    slot_pixels = lax.all_to_all(patches, "var", 2, 0, tiled=True)
    live_slot = live_index(slot_var, var_total)
    pixels = jnp.take(slot_pixels, live_slot, axis=0)
    pre_act = ein("vpt,vpd->vtd", pixels, patch_weight) + var_embed.astype(f32)[:, None, :]
    embedded = gelu_exact(pre_act).astype(bf16)
    slope = lax.optimization_barrier(gelu_slope(pre_act))

    raw_scores = (ein("vtd,dh->tvh", embedded, wq_hi) + ein("vtd,dh->tvh", embedded, wq_lo)) / math.sqrt(HD)
    squashed = jnp.tanh(raw_scores / score_cap)
    exp_scores = jnp.exp(score_cap * squashed)
    attn_f32 = exp_scores / jnp.sum(exp_scores, axis=1, keepdims=True)
    attn_bf = attn_f32.astype(bf16)

    same_head = jnp.arange(H)[:, None] == jnp.arange(H)[None, :]
    mixed_in = ein("tvh,vtd->thd", attn_bf, embedded)
    mix_hi, mix_lo = split(mixed_in)
    rows_both = jnp.concatenate([mix_hi, mix_lo], axis=0).reshape(2 * tok_count * H, width)
    all_heads = jnp.dot(rows_both, value_matrix, preferred_element_type=f32).reshape(2, tok_count, H, H, HD)
    pooled = (
        jnp.sum(jnp.where(same_head[None, None, :, :, None], all_heads, 0.0), axis=(0, 3))
        .astype(bf16)
        .reshape(tok_count, width)
    )
    mixed_out = jnp.dot(pooled, out_matrix, preferred_element_type=f32).astype(bf16)
    cot_t = lax.optimization_barrier(cotangent.T)
    grad_pooled = (
        jnp.dot(out_matrix, cot_t, preferred_element_type=f32)
        .T.astype(bf16)
        .reshape(tok_count, H, HD)
    )
    by_head = jnp.where(same_head[:, None, None, :], grad_pooled.transpose(1, 2, 0)[:, :, :, None], 0)
    spread_t = jnp.dot(value_matrix, by_head.reshape(width, tok_count * H).astype(bf16), preferred_element_type=f32)
    spread = spread_t.reshape(width, tok_count, H).transpose(1, 2, 0)
    spread_hi, spread_lo = split(spread)
    both = ein("vtd,thd->tvh", embedded, jnp.concatenate([spread_hi, spread_lo], axis=1))
    grad_attn = both[:, :, :H] + both[:, :, H:]
    grad_scores = attn_f32 * (grad_attn - jnp.sum(attn_f32 * grad_attn, axis=1, keepdims=True))
    grad_raw = grad_scores * (1.0 - squashed * squashed) / math.sqrt(HD)
    raw_hi, raw_lo = split(grad_raw)
    left = jnp.concatenate([attn_bf, attn_bf, raw_hi, raw_hi, raw_lo], axis=2)
    wq_t = jnp.concatenate([wq_hi.T, wq_lo.T, wq_hi.T], axis=0)
    right = jnp.concatenate(
        [spread_hi, spread_lo, jnp.broadcast_to(wq_t[None], (tok_count,) + wq_t.shape)], axis=1
    )
    grad_embed = ein("tvk,tkd->vtd", left, right).astype(bf16)
    grad_pre = grad_embed.astype(f32) * slope
    partial = jnp.einsum(
        "vpt,vtd->vpd", pixels.astype(f32), grad_pre, precision=lax.Precision.HIGHEST
    ).reshape(var_total, pixels_per * width)

    slots = n_var * local_slots
    cols = partial.shape[1] // n_tok
    safe = jnp.clip(slot_var, 0, var_total - 1)
    slot_rows = jnp.where((slot_var >= 0)[:, None], jnp.take(partial, safe, axis=0), 0.0)
    blocks = slot_rows.reshape(n_var, local_slots, n_tok, cols)
    by_var = lax.all_to_all(blocks, "var", 0, 0, tiled=True).sum(axis=0)
    by_tok = lax.all_to_all(by_var.transpose(1, 0, 2), "tok", 0, 0, tiled=True).sum(axis=0)
    del slots
    return (mixed_out, by_tok)


def inner_ring(mesh, n_tok):
    try:
        row = mesh.devices[0]
        slow = [tuple(d.coords)[0] for d in row]
        size = next((i for i in range(1, n_tok) if slow[i] != slow[0]), n_tok)
        if n_tok % size == 0:
            return size
    except (AttributeError, TypeError, IndexError):
        pass
    return n_tok


def solution(mesh):
    import functools

    n_tok = mesh.shape["tok"]
    n_tok_z = inner_ring(mesh, n_tok)
    fn = functools.partial(body, n_var=mesh.shape["var"], n_tok=n_tok, n_tok_x=n_tok // n_tok_z, n_tok_z=n_tok_z)
    return jax.shard_map(
        fn,
        mesh=mesh,
        in_specs=(
            P("var", None, "tok"),
            P(),
            P(),
            P(),
            P(),
            P("tok", None),
            P("tok", None),
            P("tok", None),
            P(("tok", "var"), None),
        ),
        out_specs=(P(("tok", "var"), None), P("var", "tok")),
        check_vma=False,
    )
```
